32 devices in a mesh: row: 4 (over y, core), col: 8 (over z, x).
Axes of the slice: x: 2, y: 2, z: 4, core: 2. Of those that a mesh axis runs over, the one named last changes fastest.
Arguments:
- block_x: float32 [64, 24576], P(None, ('row', 'col')), may hold values from -6 to 6
- block_p: float32 [64, 24576], P(None, ('row', 'col')), may hold values from -6 to 6
- tile_rows: int32 [4, 8, 576], P('row', 'col'), may hold values from 0 to 47, as said below
- tile_cols: int32 [4, 8, 576], P('row', 'col'), may hold values from 0 to 23, as said below
- tile_count: int32 [4, 8], P('row', 'col'), may hold values from 1 to 576, as said below
- tile_vals: bfloat16 [4, 8, 576, 128, 128], P('row', 'col'), may hold values from -0.125 to 0.125
Outputs:
- residual: float32 [64, 24576], P(None, ('row', 'col'))
- image_r: float32 [64, 24576], P(None, ('row', 'col'))
- gram_a: float32 [192, 192], replicated
- gram_b: float32 [192, 192], replicated
The draws below stay inside these ranges and needn't reach their ends.
Inputs may be any that keep to these rules, and one draw needn't show every extreme that they name: `tile_rows`: within one grid cell the live slots name distinct tiles, all with i <= j; slots at and beyond the cell's count are ignored. `tile_cols`: paired with tile_rows slot by slot. `tile_count`: some grid cell is full in every draw.
All inputs are finite; a program needn't handle non-finite values.
Results may differ from the reference program's by a relative error of at most 0.0035.
Values may be sent and summed in bfloat16 or wider, within the bound.
No kernel may reach another device: no remote copies, remote signals or barrier semaphores. Data moves between devices by JAX's collectives and lax.ppermute only.
A program may use at most 128 MiB of HBM per device.

```python
import jax
import jax.numpy as jnp
from jax import lax

K = 64
TILE = 128
XB = 6
TILES_DEV = 576
NODES = 24576
N_ROW = 4
N_COL = 8


def tile_lists(key):
    row_span = N_COL * XB
    col_span = N_ROW * XB
    candidates = row_span * col_span
    position = jnp.arange(candidates, dtype=jnp.int32)
    local_row = position // col_span
    local_col = position % col_span
    device = jnp.arange(N_ROW * N_COL, dtype=jnp.int32)

    def one_cell(cell):
        grid_row = cell // N_COL
        grid_col = cell % N_COL
        block_row = grid_row * row_span + local_row
        block_col = local_col // XB * row_span + grid_col * XB + local_col % XB
        upper = (block_row <= block_col).astype(jnp.int32)
        shuffled = jax.random.permutation(jax.random.fold_in(key, cell), candidates)
        ranking = jnp.argsort(1 - upper[shuffled], stable=True)
        picked = shuffled[ranking][:TILES_DEV]
        return (local_row[picked], local_col[picked], jnp.sum(upper))
    rows_out, cols_out, upper_total = jax.vmap(one_cell)(device)
    target = TILES_DEV * (2 * (N_ROW - device // N_COL) - 1) // (2 * N_ROW - 1)
    jitter = jax.random.randint(jax.random.fold_in(key, 7001), (N_ROW * N_COL,), 0, 1 << 20) % (target // 4 + 1)
    counts = jnp.clip(target - jitter, 1, upper_total)
    busiest = jax.random.randint(jax.random.fold_in(key, 7002), (), 0, N_COL)
    counts = jnp.where(device == busiest, TILES_DEV, counts)
    counts = jnp.minimum(counts, upper_total).astype(jnp.int32)
    return (rows_out.reshape(N_ROW, N_COL, TILES_DEV).astype(jnp.int32), cols_out.reshape(N_ROW, N_COL, TILES_DEV).astype(jnp.int32), counts.reshape(N_ROW, N_COL))


def draw_tile_rows(key, part):
    return tile_lists(key)[0]


def draw_tile_cols(key, part):
    return tile_lists(key)[1]


def draw_tile_count(key, part):
    return tile_lists(key)[2]


def level_of(stream_key, dims, shards, smallest, top_value):
    level = 1.0
    for dim, shards_of in shards:
        steps = jax.random.uniform(jax.random.fold_in(jax.random.fold_in(stream_key, 6), dim), (shards_of,), jnp.float32, smallest / len(shards), top_value / len(shards))
        level = level * jnp.repeat(jnp.exp(steps), dims[dim] // shards_of).reshape((-1,) + (1,) * (len(dims) - 1 - dim))
    return level


def scatter_about(stream_key, shape, scale, bound, shards=(), held_as=jnp.bfloat16):
    result = scale * jax.random.normal(stream_key, shape, jnp.float32)
    if shards:
        result = result * level_of(stream_key, shape, shards, -0.22, 0.18)
    return jnp.clip(result, -bound, bound).astype(held_as)


def setup_inputs(seed: int = 0) -> dict:
    arg_keys = jax.random.split(jax.random.key(seed), 7)
    block_x = scatter_about(arg_keys[0], (K, NODES), 1.0, 6.0, ((1, 32),), jnp.float32)
    block_p = scatter_about(arg_keys[1], (K, NODES), 1.0, 6.0, ((1, 32),), jnp.float32)
    tile_rows = draw_tile_rows(jax.random.fold_in(arg_keys[6], 71), 0)
    tile_cols = draw_tile_cols(jax.random.fold_in(arg_keys[6], 71), 0)
    tile_count = draw_tile_count(jax.random.fold_in(arg_keys[6], 71), 0)
    tile_vals = scatter_about(arg_keys[5], (N_ROW, N_COL, TILES_DEV, TILE, TILE), ((TILE * TILES_DEV // XB) ** (0 - 0.5)), 0.125, ((0, 4), (1, 8)))
    return dict(block_x=block_x, block_p=block_p, tile_rows=tile_rows, tile_cols=tile_cols, tile_count=tile_count, tile_vals=tile_vals)


def graph_apply(vectors, tile_rows, tile_cols, tile_count, tile_vals):
    vec_width = vectors.shape[0]
    node_count = vectors.shape[1]
    block_total = node_count // TILE
    blocks = vectors.astype(jnp.float32).reshape(vec_width, block_total, TILE)
    row_span = N_COL * XB
    slots = jnp.arange(TILES_DEV, dtype=jnp.int32)

    def visit(totals, device):
        grid_row = device // N_COL
        grid_col = device % N_COL
        local_row = tile_rows[grid_row, grid_col]
        local_col = tile_cols[grid_row, grid_col]
        block_row = (grid_row * row_span + local_row).astype(jnp.int32)
        block_col = (local_col // XB * row_span + grid_col * XB + local_col % XB).astype(jnp.int32)
        live_slots = (slots < tile_count[grid_row, grid_col]).astype(jnp.float32)
        values = tile_vals[grid_row, grid_col].astype(jnp.float32) * live_slots[:, None, None]
        col_inputs = jnp.take(blocks, block_col, axis=1)
        row_inputs = jnp.take(blocks, block_row, axis=1)
        forward = jnp.einsum('wgb,gab->wga', col_inputs, values)
        backward = jnp.einsum('wga,gab->wgb', row_inputs, values)
        totals = totals.at[:, block_row].add(forward)
        totals = totals.at[:, block_col].add(backward)
        return (totals, None)
    start_totals = jnp.zeros((vec_width, block_total, TILE), jnp.float32)
    totals, unused = lax.scan(visit, start_totals, jnp.arange(N_ROW * N_COL, dtype=jnp.int32))
    return totals.reshape(vec_width, node_count)

def reference(block_x, block_p, tile_rows, tile_cols, tile_count, tile_vals):
    highest = lax.Precision.HIGHEST
    node_count = block_x.shape[1]
    gram_x = jnp.dot(block_x.astype(jnp.float32), block_x.T.astype(jnp.float32), precision=highest, preferred_element_type=jnp.float32) / node_count
    cholesky_factor = jnp.linalg.cholesky(gram_x)
    orthonormal = lax.linalg.triangular_solve(cholesky_factor, block_x, left_side=True, lower=True)
    ortho_low = orthonormal.astype(jnp.bfloat16)
    dir_low = block_p.astype(jnp.bfloat16)
    image_x = graph_apply(ortho_low, tile_rows, tile_cols, tile_count, tile_vals)
    image_p = graph_apply(dir_low, tile_rows, tile_cols, tile_count, tile_vals)
    rayleigh = jnp.dot(orthonormal.astype(jnp.float32), image_x.T.astype(jnp.float32), precision=highest, preferred_element_type=jnp.float32) / node_count
    residual = image_x - jnp.dot(rayleigh.T.astype(jnp.float32), orthonormal.astype(jnp.float32), precision=highest, preferred_element_type=jnp.float32)
    residual_low = residual.astype(jnp.bfloat16)
    image_r = graph_apply(residual_low, tile_rows, tile_cols, tile_count, tile_vals)
    basis = jnp.concatenate([orthonormal, residual, block_p], axis=0)
    images = jnp.concatenate([image_x, image_r, image_p], axis=0)
    gram_a = jnp.dot(basis.astype(jnp.float32), images.T.astype(jnp.float32), precision=highest, preferred_element_type=jnp.float32) / node_count
    gram_b = jnp.dot(basis.astype(jnp.float32), basis.T.astype(jnp.float32), precision=highest, preferred_element_type=jnp.float32) / node_count
    return (residual, image_r, gram_a, gram_b)
```

```python
import functools

import jax
import jax.numpy as jnp
from jax import lax
from jax.experimental import pallas as pl
from jax.experimental.pallas import tpu as pltpu
from jax.sharding import PartitionSpec as P

GROUP = 64


def tile_kernel(rows_ref, cols_ref, cnt_ref, vals_ref, rin_ref, cin_ref, rout_ref, cout_ref):
    g = pl.program_id(0)
    group = vals_ref.shape[0]

    @pl.when(g == 0)
    def _():
        rout_ref[...] = jnp.zeros_like(rout_ref)
        cout_ref[...] = jnp.zeros_like(cout_ref)

    base = g * group
    live = cnt_ref[0]

    def body(t, carry):
        slot = base + t

        @pl.when(slot < live)
        def _():
            a = rows_ref[slot]
            b = cols_ref[slot]
            v = vals_ref[t]
            fwd = lax.dot_general(
                cin_ref[b], v, (((1,), (1,)), ((), ())), preferred_element_type=jnp.float32
            )
            bwd = jnp.dot(rin_ref[a], v, preferred_element_type=jnp.float32)
            rout_ref[a] += fwd
            cout_ref[b] += bwd

        return carry

    lax.fori_loop(0, group, body, 0)


def tile_products(row_blocks, col_blocks, tile_rows, tile_cols, live_count, tile_vals):
    n_rows, width, tile = row_blocks.shape
    n_cols = col_blocks.shape[0]
    slots = tile_vals.shape[0]
    group = GROUP if slots % GROUP == 0 else slots
    steps = slots // group

    def vals_map(g, rows, cols, cnt):
        last = jnp.maximum(cnt[0] - 1, 0) // group
        return (jnp.minimum(g, last), 0, 0)

    grid_spec = pltpu.PrefetchScalarGridSpec(
        num_scalar_prefetch=3,
        grid=(steps,),
        in_specs=[
            pl.BlockSpec((group, tile, tile), vals_map),
            pl.BlockSpec((n_rows, width, tile), lambda g, r, c, n: (0, 0, 0)),
            pl.BlockSpec((n_cols, width, tile), lambda g, r, c, n: (0, 0, 0)),
        ],
        out_specs=[
            pl.BlockSpec((n_rows, width, tile), lambda g, r, c, n: (0, 0, 0)),
            pl.BlockSpec((n_cols, width, tile), lambda g, r, c, n: (0, 0, 0)),
        ],
    )
    flops = 4 * slots * width * tile * tile
    bytes_accessed = (
        tile_vals.size * 2 + (row_blocks.size + col_blocks.size) * 2
        + (row_blocks.size + col_blocks.size) * 4
    )
    return pl.pallas_call(
        tile_kernel,
        grid_spec=grid_spec,
        out_shape=[
            jax.ShapeDtypeStruct((n_rows, width, tile), jnp.float32),
            jax.ShapeDtypeStruct((n_cols, width, tile), jnp.float32),
        ],
        compiler_params=pltpu.CompilerParams(
            dimension_semantics=("arbitrary",), vmem_limit_bytes=48 * 1024 * 1024
        ),
        cost_estimate=pl.CostEstimate(
            flops=flops, bytes_accessed=bytes_accessed, transcendentals=0
        ),
    )(tile_rows, tile_cols, live_count.reshape(1), tile_vals, row_blocks, col_blocks)


def apply_graph(vectors, tile_rows, tile_cols, live_count, tile_vals):
    vec_width, local_nodes = vectors.shape
    tile = tile_vals.shape[-1]
    local = vectors.reshape(vec_width, local_nodes // tile, tile).transpose(1, 0, 2)
    row_blocks = lax.all_gather(local, "col", axis=0, tiled=True)
    col_blocks = lax.all_gather(local, "row", axis=0, tiled=True)
    row_totals, col_totals = tile_products(
        row_blocks, col_blocks, tile_rows, tile_cols, live_count, tile_vals
    )
    own_rows = lax.psum_scatter(row_totals, "col", scatter_dimension=0, tiled=True)
    own_cols = lax.psum_scatter(col_totals, "row", scatter_dimension=0, tiled=True)
    return (own_rows + own_cols).transpose(1, 0, 2).reshape(vec_width, local_nodes)


def per_device(block_x, block_p, tile_rows, tile_cols, tile_count, tile_vals):
    highest = lax.Precision.HIGHEST
    width_k = block_x.shape[0]
    node_count = block_x.shape[1] * lax.axis_size("row") * lax.axis_size("col")
    slot_rows = tile_rows[0, 0]
    slot_cols = tile_cols[0, 0]
    live_count = tile_count[0, 0]
    slot_vals = tile_vals[0, 0]

    def product(left, right):
        return (
            jnp.dot(left, right.T, precision=highest, preferred_element_type=jnp.float32)
            / node_count
        )

    gram_x = lax.psum(product(block_x, block_x), ("row", "col"))
    cholesky_factor = jnp.linalg.cholesky(gram_x)
    orthonormal = lax.linalg.triangular_solve(cholesky_factor, block_x, left_side=True, lower=True)
    ortho_low = orthonormal.astype(jnp.bfloat16)
    dir_low = block_p.astype(jnp.bfloat16)
    both_images = apply_graph(
        jnp.concatenate([ortho_low, dir_low], axis=0), slot_rows, slot_cols, live_count, slot_vals
    )
    image_x = both_images[:width_k]
    image_p = both_images[width_k:]
    rayleigh = lax.psum(product(orthonormal, image_x), ("row", "col"))
    residual = image_x - jnp.dot(
        rayleigh.T, orthonormal, precision=highest, preferred_element_type=jnp.float32
    )
    residual_low = residual.astype(jnp.bfloat16)
    image_r = apply_graph(residual_low, slot_rows, slot_cols, live_count, slot_vals)
    basis = jnp.concatenate([orthonormal, residual, block_p], axis=0)
    images = jnp.concatenate([image_x, image_r, image_p], axis=0)
    gram_a, gram_b = lax.psum((product(basis, images), product(basis, basis)), ("row", "col"))
    return (residual, image_r, gram_a, gram_b)


def solution(mesh):
    in_specs = (
        P(None, ("row", "col")),
        P(None, ("row", "col")),
        P("row", "col", None),
        P("row", "col", None),
        P("row", "col"),
        P("row", "col", None, None, None),
    )
    out_specs = (P(None, ("row", "col")), P(None, ("row", "col")), P(), P())
    return jax.shard_map(
        per_device, mesh=mesh, in_specs=in_specs, out_specs=out_specs, check_vma=False
    )
```

```python
import functools

import jax
import jax.numpy as jnp
from jax import lax
from jax.experimental import pallas as pl
from jax.experimental.pallas import tpu as pltpu
from jax.sharding import PartitionSpec as P

GROUP = 64


def tile_kernel(rows_ref, cols_ref, cnt_ref, vals_ref, rin_ref, cin_ref, rout_ref, cout_ref):
    g = pl.program_id(0)
    group = vals_ref.shape[0]

    @pl.when(g == 0)
    def _():
        rout_ref[...] = jnp.zeros_like(rout_ref)
        cout_ref[...] = jnp.zeros_like(cout_ref)

    base = g * group
    live = cnt_ref[0]

    def body(t, carry):
        slot = base + t

        @pl.when(slot < live)
        def _():
            a = rows_ref[slot]
            b = cols_ref[slot]
            v = vals_ref[t]
            fwd = lax.dot_general(
                cin_ref[b], v, (((1,), (1,)), ((), ())), preferred_element_type=jnp.float32
            )
            bwd = jnp.dot(rin_ref[a], v, preferred_element_type=jnp.float32)
            rout_ref[a] += fwd
            cout_ref[b] += bwd

        return carry

    lax.fori_loop(0, group, body, 0)


def tile_products(row_blocks, col_blocks, tile_rows, tile_cols, live_count, tile_vals):
    n_rows, width, tile = row_blocks.shape
    n_cols = col_blocks.shape[0]
    slots = tile_vals.shape[0]
    group = GROUP if slots % GROUP == 0 else slots
    steps = slots // group

    def vals_map(g, rows, cols, cnt):
        last = jnp.maximum(cnt[0] - 1, 0) // group
        return (jnp.minimum(g, last), 0, 0)

    grid_spec = pltpu.PrefetchScalarGridSpec(
        num_scalar_prefetch=3,
        grid=(steps,),
        in_specs=[
            pl.BlockSpec((group, tile, tile), vals_map),
            pl.BlockSpec((n_rows, width, tile), lambda g, r, c, n: (0, 0, 0)),
            pl.BlockSpec((n_cols, width, tile), lambda g, r, c, n: (0, 0, 0)),
        ],
        out_specs=[
            pl.BlockSpec((n_rows, width, tile), lambda g, r, c, n: (0, 0, 0)),
            pl.BlockSpec((n_cols, width, tile), lambda g, r, c, n: (0, 0, 0)),
        ],
    )
    flops = 4 * slots * width * tile * tile
    bytes_accessed = (
        tile_vals.size * 2 + (row_blocks.size + col_blocks.size) * 2
        + (row_blocks.size + col_blocks.size) * 4
    )
    return pl.pallas_call(
        tile_kernel,
        grid_spec=grid_spec,
        out_shape=[
            jax.ShapeDtypeStruct((n_rows, width, tile), jnp.float32),
            jax.ShapeDtypeStruct((n_cols, width, tile), jnp.float32),
        ],
        compiler_params=pltpu.CompilerParams(
            dimension_semantics=("arbitrary",), vmem_limit_bytes=48 * 1024 * 1024
        ),
        cost_estimate=pl.CostEstimate(
            flops=flops, bytes_accessed=bytes_accessed, transcendentals=0
        ),
    )(tile_rows, tile_cols, live_count.reshape(1), tile_vals, row_blocks, col_blocks)


def exchange_pairs(size, step):
    return [(i, i ^ step) for i in range(size)]


def reversed_bits(value, bits):
    result = jnp.zeros_like(value)
    for k in range(bits):
        result = result | (((value >> k) & 1) << (bits - 1 - k))
    return result


def gather_blocks(local, axis):
    size = lax.axis_size(axis)
    held = local
    step = size // 2
    while step >= 1:
        held = jnp.concatenate([held, lax.ppermute(held, axis, exchange_pairs(size, step))], axis=0)
        step //= 2
    return held


def scatter_sum(totals, axis):
    size = lax.axis_size(axis)
    held = totals
    step = 1
    while step < size:
        half = held.shape[0] // 2
        held = held[:half] + lax.ppermute(held[half:], axis, exchange_pairs(size, step))
        step *= 2
    return held


def all_sum(value):
    for axis in ("row", "col"):
        size = lax.axis_size(axis)
        step = 1
        while step < size:
            value = value + lax.ppermute(value, axis, exchange_pairs(size, step))
            step *= 2
    return value


def held_position(index, axis, blocks_each):
    size = lax.axis_size(axis)
    bits = size.bit_length() - 1
    me = lax.axis_index(axis)
    owner = index // blocks_each
    return reversed_bits(me ^ owner, bits) * blocks_each + index % blocks_each


def apply_graph(vectors, tile_rows, tile_cols, live_count, tile_vals):
    vec_width, local_nodes = vectors.shape
    tile = tile_vals.shape[-1]
    blocks_each = local_nodes // tile
    local = vectors.reshape(vec_width, blocks_each, tile).transpose(1, 0, 2)
    row_blocks = gather_blocks(local, "col")
    col_blocks = gather_blocks(local, "row")
    row_totals, col_totals = tile_products(
        row_blocks, col_blocks, tile_rows, tile_cols, live_count, tile_vals
    )
    own_rows = scatter_sum(row_totals, "col")
    own_cols = scatter_sum(col_totals, "row")
    return (own_rows + own_cols).transpose(1, 0, 2).reshape(vec_width, local_nodes)


def per_device(block_x, block_p, tile_rows, tile_cols, tile_count, tile_vals):
    highest = lax.Precision.HIGHEST
    width_k = block_x.shape[0]
    node_count = block_x.shape[1] * lax.axis_size("row") * lax.axis_size("col")
    blocks_each = block_x.shape[1] // tile_vals.shape[-1]
    slot_rows = held_position(tile_rows[0, 0], "col", blocks_each)
    slot_cols = held_position(tile_cols[0, 0], "row", blocks_each)
    live_count = tile_count[0, 0]
    slot_vals = tile_vals[0, 0]

    def product(left, right):
        return (
            jnp.dot(left, right.T, precision=highest, preferred_element_type=jnp.float32)
            / node_count
        )

    gram_x = all_sum(product(block_x, block_x))
    cholesky_factor = jnp.linalg.cholesky(gram_x)
    orthonormal = lax.linalg.triangular_solve(cholesky_factor, block_x, left_side=True, lower=True)
    ortho_low = orthonormal.astype(jnp.bfloat16)
    dir_low = block_p.astype(jnp.bfloat16)
    both_images = apply_graph(
        jnp.concatenate([ortho_low, dir_low], axis=0), slot_rows, slot_cols, live_count, slot_vals
    )
    image_x = both_images[:width_k]
    image_p = both_images[width_k:]
    rayleigh = all_sum(product(orthonormal, image_x))
    residual = image_x - jnp.dot(
        rayleigh.T, orthonormal, precision=highest, preferred_element_type=jnp.float32
    )
    residual_low = residual.astype(jnp.bfloat16)
    image_r = apply_graph(residual_low, slot_rows, slot_cols, live_count, slot_vals)
    basis = jnp.concatenate([orthonormal, residual, block_p], axis=0)
    images = jnp.concatenate([image_x, image_r, image_p], axis=0)
    gram_a, gram_b = all_sum(jnp.stack([product(basis, images), product(basis, basis)]))
    return (residual, image_r, gram_a, gram_b)


def solution(mesh):
    in_specs = (
        P(None, ("row", "col")),
        P(None, ("row", "col")),
        P("row", "col", None),
        P("row", "col", None),
        P("row", "col"),
        P("row", "col", None, None, None),
    )
    out_specs = (P(None, ("row", "col")), P(None, ("row", "col")), P(), P())
    return jax.shard_map(
        per_device, mesh=mesh, in_specs=in_specs, out_specs=out_specs, check_vma=False
    )
```

```python
import functools

import jax
import jax.numpy as jnp
from jax import lax
from jax.experimental import pallas as pl
from jax.experimental.pallas import tpu as pltpu
from jax.sharding import PartitionSpec as P

GROUP = 64
UNROLL = 32


def tile_kernel(rows_ref, cols_ref, cnt_ref, vals_ref, rin_ref, cin_ref, rout_ref, cout_ref):
    g = pl.program_id(0)
    group = vals_ref.shape[0]

    @pl.when(g == 0)
    def _():
        rout_ref[...] = jnp.zeros_like(rout_ref)
        cout_ref[...] = jnp.zeros_like(cout_ref)

    base = g * group
    live = cnt_ref[0]

    def tile_step(t):
        slot = base + t
        a = rows_ref[slot]
        b = cols_ref[slot]
        v = vals_ref[t]
        fwd = lax.dot_general(
            cin_ref[b], v, (((1,), (1,)), ((), ())), preferred_element_type=jnp.float32
        )
        bwd = jnp.dot(rin_ref[a], v, preferred_element_type=jnp.float32)
        rout_ref[a] += fwd
        cout_ref[b] += bwd

    def full_body(t, carry):
        tile_step(t)
        return carry

    def part_body(t, carry):
        @pl.when(base + t < live)
        def _():
            tile_step(t)

        return carry

    @pl.when(base + group <= live)
    def _():
        lax.fori_loop(0, group, full_body, 0, unroll=UNROLL)

    @pl.when(jnp.logical_and(base < live, base + group > live))
    def _():
        lax.fori_loop(0, group, part_body, 0)


def tile_products(row_blocks, col_blocks, tile_rows, tile_cols, live_count, tile_vals):
    n_rows, width, tile = row_blocks.shape
    n_cols = col_blocks.shape[0]
    slots = tile_vals.shape[0]
    group = GROUP if slots % GROUP == 0 else slots
    steps = slots // group

    def vals_map(g, rows, cols, cnt):
        last = jnp.maximum(cnt[0] - 1, 0) // group
        return (jnp.minimum(g, last), 0, 0)

    grid_spec = pltpu.PrefetchScalarGridSpec(
        num_scalar_prefetch=3,
        grid=(steps,),
        in_specs=[
            pl.BlockSpec((group, tile, tile), vals_map),
            pl.BlockSpec((n_rows, width, tile), lambda g, r, c, n: (0, 0, 0)),
            pl.BlockSpec((n_cols, width, tile), lambda g, r, c, n: (0, 0, 0)),
        ],
        out_specs=[
            pl.BlockSpec((n_rows, width, tile), lambda g, r, c, n: (0, 0, 0)),
            pl.BlockSpec((n_cols, width, tile), lambda g, r, c, n: (0, 0, 0)),
        ],
    )
    flops = 4 * slots * width * tile * tile
    bytes_accessed = (
        tile_vals.size * 2 + (row_blocks.size + col_blocks.size) * 2
        + (row_blocks.size + col_blocks.size) * 4
    )
    return pl.pallas_call(
        tile_kernel,
        grid_spec=grid_spec,
        out_shape=[
            jax.ShapeDtypeStruct((n_rows, width, tile), jnp.float32),
            jax.ShapeDtypeStruct((n_cols, width, tile), jnp.float32),
        ],
        compiler_params=pltpu.CompilerParams(
            dimension_semantics=("arbitrary",), vmem_limit_bytes=48 * 1024 * 1024
        ),
        cost_estimate=pl.CostEstimate(
            flops=flops, bytes_accessed=bytes_accessed, transcendentals=0
        ),
    )(tile_rows, tile_cols, live_count.reshape(1), tile_vals, row_blocks, col_blocks)


def exchange_pairs(size, step):
    return [(i, i ^ step) for i in range(size)]


def reversed_bits(value, bits):
    result = jnp.zeros_like(value)
    for k in range(bits):
        result = result | (((value >> k) & 1) << (bits - 1 - k))
    return result


def gather_blocks(local, axis):
    size = lax.axis_size(axis)
    held = local
    step = size // 2
    while step >= 1:
        held = jnp.concatenate([held, lax.ppermute(held, axis, exchange_pairs(size, step))], axis=0)
        step //= 2
    return held


def scatter_sum(totals, axis):
    size = lax.axis_size(axis)
    held = totals
    step = 1
    while step < size:
        half = held.shape[0] // 2
        held = held[:half] + lax.ppermute(held[half:], axis, exchange_pairs(size, step))
        step *= 2
    return held


def all_sum(value):
    for axis in ("row", "col"):
        size = lax.axis_size(axis)
        step = 1
        while step < size:
            value = value + lax.ppermute(value, axis, exchange_pairs(size, step))
            step *= 2
    return value


def held_position(index, axis, blocks_each):
    size = lax.axis_size(axis)
    bits = size.bit_length() - 1
    me = lax.axis_index(axis)
    owner = index // blocks_each
    return reversed_bits(me ^ owner, bits) * blocks_each + index % blocks_each


def apply_graph(vectors, tile_rows, tile_cols, live_count, tile_vals):
    vec_width, local_nodes = vectors.shape
    tile = tile_vals.shape[-1]
    blocks_each = local_nodes // tile
    local = vectors.reshape(vec_width, blocks_each, tile).transpose(1, 0, 2)
    row_blocks = gather_blocks(local, "col")
    col_blocks = gather_blocks(local, "row")
    row_totals, col_totals = tile_products(
        row_blocks, col_blocks, tile_rows, tile_cols, live_count, tile_vals
    )
    own_rows = scatter_sum(row_totals, "col")
    own_cols = scatter_sum(col_totals, "row")
    return (own_rows + own_cols).transpose(1, 0, 2).reshape(vec_width, local_nodes)


def per_device(block_x, block_p, tile_rows, tile_cols, tile_count, tile_vals):
    highest = lax.Precision.HIGHEST
    width_k = block_x.shape[0]
    node_count = block_x.shape[1] * lax.axis_size("row") * lax.axis_size("col")
    blocks_each = block_x.shape[1] // tile_vals.shape[-1]
    slot_rows = held_position(tile_rows[0, 0], "col", blocks_each)
    slot_cols = held_position(tile_cols[0, 0], "row", blocks_each)
    live_count = tile_count[0, 0]
    slot_vals = tile_vals[0, 0]

    def product(left, right):
        return (
            jnp.dot(left, right.T, precision=highest, preferred_element_type=jnp.float32)
            / node_count
        )

    gram_x = all_sum(product(block_x, block_x))
    cholesky_factor = jnp.linalg.cholesky(gram_x)
    orthonormal = lax.linalg.triangular_solve(cholesky_factor, block_x, left_side=True, lower=True)
    ortho_low = orthonormal.astype(jnp.bfloat16)
    dir_low = block_p.astype(jnp.bfloat16)
    both_images = apply_graph(
        jnp.concatenate([ortho_low, dir_low], axis=0), slot_rows, slot_cols, live_count, slot_vals
    )
    image_x = both_images[:width_k]
    image_p = both_images[width_k:]
    rayleigh = all_sum(product(orthonormal, image_x))
    residual = image_x - jnp.dot(
        rayleigh.T, orthonormal, precision=highest, preferred_element_type=jnp.float32
    )
    residual_low = residual.astype(jnp.bfloat16)
    image_r = apply_graph(residual_low, slot_rows, slot_cols, live_count, slot_vals)
    basis = jnp.concatenate([orthonormal, residual, block_p], axis=0)
    images = jnp.concatenate([image_x, image_r, image_p], axis=0)
    gram_a, gram_b = all_sum(jnp.stack([product(basis, images), product(basis, basis)]))
    return (residual, image_r, gram_a, gram_b)


def solution(mesh):
    in_specs = (
        P(None, ("row", "col")),
        P(None, ("row", "col")),
        P("row", "col", None),
        P("row", "col", None),
        P("row", "col"),
        P("row", "col", None, None, None),
    )
    out_specs = (P(None, ("row", "col")), P(None, ("row", "col")), P(), P())
    return jax.shard_map(
        per_device, mesh=mesh, in_specs=in_specs, out_specs=out_specs, check_vma=False
    )
```

```python
import functools

import jax
import jax.numpy as jnp
from jax import lax
from jax.experimental import pallas as pl
from jax.experimental.pallas import tpu as pltpu
from jax.sharding import PartitionSpec as P

GROUP = 64
UNROLL = 32


def tile_kernel(rows_ref, cols_ref, cnt_ref, vals_ref, rin_ref, cin_ref, *out_refs):
    g = pl.program_id(0)
    group = vals_ref.shape[0]
    row_outs = out_refs[0::2]
    col_outs = out_refs[1::2]
    edges = [0]
    for ref in row_outs:
        edges.append(edges[-1] + ref.shape[1])

    @pl.when(g == 0)
    def _():
        for ref in out_refs:
            ref[...] = jnp.zeros_like(ref)

    base = g * group
    live = cnt_ref[0]

    def tile_step(t):
        slot = base + t
        a = rows_ref[slot]
        b = cols_ref[slot]
        v = vals_ref[t]
        fwd = lax.dot_general(
            cin_ref[b], v, (((1,), (1,)), ((), ())), preferred_element_type=jnp.float32
        )
        bwd = jnp.dot(rin_ref[a], v, preferred_element_type=jnp.float32)
        for k in range(len(row_outs)):
            row_outs[k][a] += fwd[edges[k]:edges[k + 1]]
            col_outs[k][b] += bwd[edges[k]:edges[k + 1]]

    def full_body(t, carry):
        tile_step(t)
        return carry

    def part_body(t, carry):
        @pl.when(base + t < live)
        def _():
            tile_step(t)

        return carry

    @pl.when(base + group <= live)
    def _():
        lax.fori_loop(0, group, full_body, 0, unroll=UNROLL)

    @pl.when(jnp.logical_and(base < live, base + group > live))
    def _():
        lax.fori_loop(0, group, part_body, 0)


def tile_products(row_blocks, col_blocks, tile_rows, tile_cols, live_count, tile_vals, widths):
    n_rows, width, tile = row_blocks.shape
    n_cols = col_blocks.shape[0]
    slots = tile_vals.shape[0]
    group = GROUP if slots % GROUP == 0 else slots
    steps = slots // group

    def vals_map(g, rows, cols, cnt):
        last = jnp.maximum(cnt[0] - 1, 0) // group
        return (jnp.minimum(g, last), 0, 0)

    grid_spec = pltpu.PrefetchScalarGridSpec(
        num_scalar_prefetch=3,
        grid=(steps,),
        in_specs=[
            pl.BlockSpec((group, tile, tile), vals_map),
            pl.BlockSpec((n_rows, width, tile), lambda g, r, c, n: (0, 0, 0)),
            pl.BlockSpec((n_cols, width, tile), lambda g, r, c, n: (0, 0, 0)),
        ],
        out_specs=[
            pl.BlockSpec((n, w, tile), lambda g, r, c, k: (0, 0, 0))
            for w in widths
            for n in (n_rows, n_cols)
        ],
    )
    flops = 4 * slots * width * tile * tile
    bytes_accessed = (
        tile_vals.size * 2 + (row_blocks.size + col_blocks.size) * 2
        + (row_blocks.size + col_blocks.size) * 4
    )
    return pl.pallas_call(
        tile_kernel,
        grid_spec=grid_spec,
        out_shape=[
            jax.ShapeDtypeStruct((n, w, tile), jnp.float32) for w in widths for n in (n_rows, n_cols)
        ],
        compiler_params=pltpu.CompilerParams(
            dimension_semantics=("arbitrary",), vmem_limit_bytes=48 * 1024 * 1024
        ),
        cost_estimate=pl.CostEstimate(
            flops=flops, bytes_accessed=bytes_accessed, transcendentals=0
        ),
    )(tile_rows, tile_cols, live_count.reshape(1), tile_vals, row_blocks, col_blocks)


def exchange_pairs(size, step):
    return [(i, i ^ step) for i in range(size)]


def reversed_bits(value, bits):
    result = jnp.zeros_like(value)
    for k in range(bits):
        result = result | (((value >> k) & 1) << (bits - 1 - k))
    return result


def gather_blocks(local, axis):
    size = lax.axis_size(axis)
    held = local
    step = size // 2
    while step >= 1:
        held = jnp.concatenate([held, lax.ppermute(held, axis, exchange_pairs(size, step))], axis=0)
        step //= 2
    return held


def scatter_sum(totals, axis):
    size = lax.axis_size(axis)
    held = totals
    step = 1
    while step < size:
        half = held.shape[0] // 2
        held = held[:half] + lax.ppermute(held[half:], axis, exchange_pairs(size, step))
        step *= 2
    return held


def all_sum(value):
    for axis in ("row", "col"):
        size = lax.axis_size(axis)
        step = 1
        while step < size:
            value = value + lax.ppermute(value, axis, exchange_pairs(size, step))
            step *= 2
    return value


def held_position(index, axis, blocks_each):
    size = lax.axis_size(axis)
    bits = size.bit_length() - 1
    me = lax.axis_index(axis)
    owner = index // blocks_each
    return reversed_bits(me ^ owner, bits) * blocks_each + index % blocks_each


def to_blocks(vectors, tile):
    vec_width, local_nodes = vectors.shape
    return vectors.reshape(vec_width, local_nodes // tile, tile).transpose(1, 0, 2)


def from_blocks(blocks):
    count, vec_width, tile = blocks.shape
    return blocks.transpose(1, 0, 2).reshape(vec_width, count * tile)


def gathered(vectors, tile):
    local = to_blocks(vectors, tile)
    return gather_blocks(local, "col"), gather_blocks(local, "row")


def owned(row_totals, col_totals):
    return from_blocks(scatter_sum(row_totals, "col") + scatter_sum(col_totals, "row"))


def per_device(block_x, block_p, tile_rows, tile_cols, tile_count, tile_vals):
    highest = lax.Precision.HIGHEST
    width_k = block_x.shape[0]
    node_count = block_x.shape[1] * lax.axis_size("row") * lax.axis_size("col")
    blocks_each = block_x.shape[1] // tile_vals.shape[-1]
    slot_rows = held_position(tile_rows[0, 0], "col", blocks_each)
    slot_cols = held_position(tile_cols[0, 0], "row", blocks_each)
    live_count = tile_count[0, 0]
    slot_vals = tile_vals[0, 0]

    def product(left, right):
        return (
            jnp.dot(left, right.T, precision=highest, preferred_element_type=jnp.float32)
            / node_count
        )

    gram_x = all_sum(product(block_x, block_x))
    cholesky_factor = jnp.linalg.cholesky(gram_x)
    orthonormal = lax.linalg.triangular_solve(cholesky_factor, block_x, left_side=True, lower=True)
    tile = tile_vals.shape[-1]
    dir_rows, dir_cols = gathered(block_p.astype(jnp.bfloat16), tile)
    ortho_rows, ortho_cols = gathered(orthonormal.astype(jnp.bfloat16), tile)
    x_rows, x_cols, p_rows, p_cols = tile_products(
        jnp.concatenate([ortho_rows, dir_rows], axis=1),
        jnp.concatenate([ortho_cols, dir_cols], axis=1),
        slot_rows, slot_cols, live_count, slot_vals, (width_k, block_p.shape[0]),
    )
    image_x = owned(x_rows, x_cols)
    rayleigh = all_sum(product(orthonormal, image_x))
    residual = image_x - jnp.dot(
        rayleigh.T, orthonormal, precision=highest, preferred_element_type=jnp.float32
    )
    res_rows, res_cols = gathered(residual.astype(jnp.bfloat16), tile)
    image_p = owned(p_rows, p_cols)
    basis = jnp.concatenate([orthonormal, residual, block_p], axis=0)
    early = all_sum(
        jnp.concatenate(
            [product(basis, basis), product(basis, image_x), product(basis, image_p)], axis=1
        )
    )
    r_rows, r_cols = tile_products(
        res_rows, res_cols, slot_rows, slot_cols, live_count, slot_vals, (residual.shape[0],)
    )
    image_r = owned(r_rows, r_cols)
    late = all_sum(product(basis, image_r))
    span = basis.shape[0]
    gram_b = early[:, :span]
    gram_a = jnp.concatenate(
        [early[:, span:span + width_k], late, early[:, span + width_k:]], axis=1
    )
    return (residual, image_r, gram_a, gram_b)


def solution(mesh):
    in_specs = (
        P(None, ("row", "col")),
        P(None, ("row", "col")),
        P("row", "col", None),
        P("row", "col", None),
        P("row", "col"),
        P("row", "col", None, None, None),
    )
    out_specs = (P(None, ("row", "col")), P(None, ("row", "col")), P(), P())
    return jax.shard_map(
        per_device, mesh=mesh, in_specs=in_specs, out_specs=out_specs, check_vma=False
    )
```

```python
import functools

import jax
import jax.numpy as jnp
from jax import lax
from jax.experimental import pallas as pl
from jax.experimental.pallas import tpu as pltpu
from jax.sharding import PartitionSpec as P

GROUP = 64
UNROLL = 32


def tile_kernel(rows_ref, cols_ref, cnt_ref, vals_ref, rin_ref, cin_ref, *out_refs):
    g = pl.program_id(0)
    group = vals_ref.shape[0]
    row_outs = out_refs[0::2]
    col_outs = out_refs[1::2]
    edges = [0]
    for ref in row_outs:
        edges.append(edges[-1] + ref.shape[1])

    @pl.when(g == 0)
    def _():
        for ref in out_refs:
            ref[...] = jnp.zeros_like(ref)

    base = g * group
    live = cnt_ref[0]

    def tile_step(t):
        slot = base + t
        a = rows_ref[slot]
        b = cols_ref[slot]
        v = vals_ref[t]
        fwd = lax.dot_general(
            cin_ref[b], v, (((1,), (1,)), ((), ())), preferred_element_type=jnp.float32
        )
        bwd = jnp.dot(rin_ref[a], v, preferred_element_type=jnp.float32)
        for k in range(len(row_outs)):
            row_outs[k][a] += fwd[edges[k]:edges[k + 1]]
            col_outs[k][b] += bwd[edges[k]:edges[k + 1]]

    def full_body(t, carry):
        tile_step(t)
        return carry

    def part_body(t, carry):
        @pl.when(base + t < live)
        def _():
            tile_step(t)

        return carry

    @pl.when(base + group <= live)
    def _():
        lax.fori_loop(0, group, full_body, 0, unroll=UNROLL)

    @pl.when(jnp.logical_and(base < live, base + group > live))
    def _():
        lax.fori_loop(0, group, part_body, 0)


def tile_products(row_blocks, col_blocks, tile_rows, tile_cols, live_count, tile_vals, widths):
    n_rows, width, tile = row_blocks.shape
    n_cols = col_blocks.shape[0]
    slots = tile_vals.shape[0]
    group = GROUP if slots % GROUP == 0 else slots
    steps = slots // group

    def vals_map(g, rows, cols, cnt):
        last = jnp.maximum(cnt[0] - 1, 0) // group
        return (jnp.minimum(g, last), 0, 0)

    grid_spec = pltpu.PrefetchScalarGridSpec(
        num_scalar_prefetch=3,
        grid=(steps,),
        in_specs=[
            pl.BlockSpec((group, tile, tile), vals_map),
            pl.BlockSpec((n_rows, width, tile), lambda g, r, c, n: (0, 0, 0)),
            pl.BlockSpec((n_cols, width, tile), lambda g, r, c, n: (0, 0, 0)),
        ],
        out_specs=[
            pl.BlockSpec((n, w, tile), lambda g, r, c, k: (0, 0, 0))
            for w in widths
            for n in (n_rows, n_cols)
        ],
    )
    flops = 4 * slots * width * tile * tile
    bytes_accessed = (
        tile_vals.size * 2 + (row_blocks.size + col_blocks.size) * 2
        + (row_blocks.size + col_blocks.size) * 4
    )
    return pl.pallas_call(
        tile_kernel,
        grid_spec=grid_spec,
        out_shape=[
            jax.ShapeDtypeStruct((n, w, tile), jnp.float32) for w in widths for n in (n_rows, n_cols)
        ],
        compiler_params=pltpu.CompilerParams(
            dimension_semantics=("arbitrary",), vmem_limit_bytes=48 * 1024 * 1024
        ),
        cost_estimate=pl.CostEstimate(
            flops=flops, bytes_accessed=bytes_accessed, transcendentals=0
        ),
    )(tile_rows, tile_cols, live_count.reshape(1), tile_vals, row_blocks, col_blocks)


def exchange_pairs(size, step):
    return [(i, i ^ step) for i in range(size)]


def reversed_bits(value, bits):
    result = jnp.zeros_like(value)
    for k in range(bits):
        result = result | (((value >> k) & 1) << (bits - 1 - k))
    return result


def gather_blocks(local, axis):
    size = lax.axis_size(axis)
    held = local
    step = size // 2
    while step >= 1:
        held = jnp.concatenate([held, lax.ppermute(held, axis, exchange_pairs(size, step))], axis=0)
        step //= 2
    return held


def scatter_sum(totals, axis):
    size = lax.axis_size(axis)
    held = totals
    step = 1
    while step < size:
        half = held.shape[0] // 2
        sent = held[half:].astype(jnp.bfloat16)
        held = held[:half] + lax.ppermute(sent, axis, exchange_pairs(size, step)).astype(held.dtype)
        step *= 2
    return held


def all_sum(value):
    for axis in ("row", "col"):
        size = lax.axis_size(axis)
        step = 1
        while step < size:
            value = value + lax.ppermute(value, axis, exchange_pairs(size, step))
            step *= 2
    return value


def held_position(index, axis, blocks_each):
    size = lax.axis_size(axis)
    bits = size.bit_length() - 1
    me = lax.axis_index(axis)
    owner = index // blocks_each
    return reversed_bits(me ^ owner, bits) * blocks_each + index % blocks_each


def to_blocks(vectors, tile):
    vec_width, local_nodes = vectors.shape
    return vectors.reshape(vec_width, local_nodes // tile, tile).transpose(1, 0, 2)


def from_blocks(blocks):
    count, vec_width, tile = blocks.shape
    return blocks.transpose(1, 0, 2).reshape(vec_width, count * tile)


def gathered(vectors, tile):
    local = to_blocks(vectors, tile)
    return gather_blocks(local, "col"), gather_blocks(local, "row")


def owned(row_totals, col_totals):
    return from_blocks(scatter_sum(row_totals, "col") + scatter_sum(col_totals, "row"))


def per_device(block_x, block_p, tile_rows, tile_cols, tile_count, tile_vals):
    highest = lax.Precision.HIGHEST
    width_k = block_x.shape[0]
    node_count = block_x.shape[1] * lax.axis_size("row") * lax.axis_size("col")
    blocks_each = block_x.shape[1] // tile_vals.shape[-1]
    slot_rows = held_position(tile_rows[0, 0], "col", blocks_each)
    slot_cols = held_position(tile_cols[0, 0], "row", blocks_each)
    live_count = tile_count[0, 0]
    slot_vals = tile_vals[0, 0]

    def product(left, right):
        return (
            jnp.dot(left, right.T, precision=highest, preferred_element_type=jnp.float32)
            / node_count
        )

    gram_x = all_sum(product(block_x, block_x))
    cholesky_factor = jnp.linalg.cholesky(gram_x)
    orthonormal = lax.linalg.triangular_solve(cholesky_factor, block_x, left_side=True, lower=True)
    tile = tile_vals.shape[-1]
    dir_rows, dir_cols = gathered(block_p.astype(jnp.bfloat16), tile)
    ortho_rows, ortho_cols = gathered(orthonormal.astype(jnp.bfloat16), tile)
    x_rows, x_cols, p_rows, p_cols = tile_products(
        jnp.concatenate([ortho_rows, dir_rows], axis=1),
        jnp.concatenate([ortho_cols, dir_cols], axis=1),
        slot_rows, slot_cols, live_count, slot_vals, (width_k, block_p.shape[0]),
    )
    image_x = owned(x_rows, x_cols)
    rayleigh = all_sum(product(orthonormal, image_x))
    residual = image_x - jnp.dot(
        rayleigh.T, orthonormal, precision=highest, preferred_element_type=jnp.float32
    )
    res_rows, res_cols = gathered(residual.astype(jnp.bfloat16), tile)
    image_p = owned(p_rows, p_cols)
    basis = jnp.concatenate([orthonormal, residual, block_p], axis=0)
    early = all_sum(
        jnp.concatenate(
            [product(basis, basis), product(basis, image_x), product(basis, image_p)], axis=1
        )
    )
    r_rows, r_cols = tile_products(
        res_rows, res_cols, slot_rows, slot_cols, live_count, slot_vals, (residual.shape[0],)
    )
    image_r = owned(r_rows, r_cols)
    late = all_sum(product(basis, image_r))
    span = basis.shape[0]
    gram_b = early[:, :span]
    gram_a = jnp.concatenate(
        [early[:, span:span + width_k], late, early[:, span + width_k:]], axis=1
    )
    return (residual, image_r, gram_a, gram_b)


def solution(mesh):
    in_specs = (
        P(None, ("row", "col")),
        P(None, ("row", "col")),
        P("row", "col", None),
        P("row", "col", None),
        P("row", "col"),
        P("row", "col", None, None, None),
    )
    out_specs = (P(None, ("row", "col")), P(None, ("row", "col")), P(), P())
    return jax.shard_map(
        per_device, mesh=mesh, in_specs=in_specs, out_specs=out_specs, check_vma=False
    )
```

```python
import functools

import jax
import jax.numpy as jnp
from jax import lax
from jax.experimental import pallas as pl
from jax.experimental.pallas import tpu as pltpu
from jax.sharding import PartitionSpec as P

GROUP = 64
UNROLL = 32


def tile_kernel(rows_ref, cols_ref, cnt_ref, vals_ref, rin_ref, cin_ref, *out_refs):
    g = pl.program_id(0)
    group = vals_ref.shape[0]
    row_outs = out_refs[0::2]
    col_outs = out_refs[1::2]
    edges = [0]
    for ref in row_outs:
        edges.append(edges[-1] + ref.shape[1])

    @pl.when(g == 0)
    def _():
        for ref in out_refs:
            ref[...] = jnp.zeros_like(ref)

    base = g * group
    live = cnt_ref[0]

    def tile_step(t):
        slot = base + t
        a = rows_ref[slot]
        b = cols_ref[slot]
        v = vals_ref[t]
        fwd = lax.dot_general(
            cin_ref[b], v, (((1,), (1,)), ((), ())), preferred_element_type=jnp.float32
        )
        bwd = jnp.dot(rin_ref[a], v, preferred_element_type=jnp.float32)
        for k in range(len(row_outs)):
            row_outs[k][a] += fwd[edges[k]:edges[k + 1]]
            col_outs[k][b] += bwd[edges[k]:edges[k + 1]]

    def full_body(t, carry):
        tile_step(t)
        return carry

    def part_body(t, carry):
        @pl.when(base + t < live)
        def _():
            tile_step(t)

        return carry

    @pl.when(base + group <= live)
    def _():
        lax.fori_loop(0, group, full_body, 0, unroll=UNROLL)

    @pl.when(jnp.logical_and(base < live, base + group > live))
    def _():
        lax.fori_loop(0, group, part_body, 0)


def tile_products(row_blocks, col_blocks, tile_rows, tile_cols, live_count, tile_vals, widths):
    n_rows, width, tile = row_blocks.shape
    n_cols = col_blocks.shape[0]
    slots = tile_vals.shape[0]
    group = GROUP if slots % GROUP == 0 else slots
    steps = slots // group

    def vals_map(g, rows, cols, cnt):
        last = jnp.maximum(cnt[0] - 1, 0) // group
        return (jnp.minimum(g, last), 0, 0)

    grid_spec = pltpu.PrefetchScalarGridSpec(
        num_scalar_prefetch=3,
        grid=(steps,),
        in_specs=[
            pl.BlockSpec((group, tile, tile), vals_map),
            pl.BlockSpec((n_rows, width, tile), lambda g, r, c, n: (0, 0, 0)),
            pl.BlockSpec((n_cols, width, tile), lambda g, r, c, n: (0, 0, 0)),
        ],
        out_specs=[
            pl.BlockSpec((n, w, tile), lambda g, r, c, k: (0, 0, 0))
            for w in widths
            for n in (n_rows, n_cols)
        ],
    )
    flops = 4 * slots * width * tile * tile
    bytes_accessed = (
        tile_vals.size * 2 + (row_blocks.size + col_blocks.size) * 2
        + (row_blocks.size + col_blocks.size) * 4
    )
    return pl.pallas_call(
        tile_kernel,
        grid_spec=grid_spec,
        out_shape=[
            jax.ShapeDtypeStruct((n, w, tile), jnp.float32) for w in widths for n in (n_rows, n_cols)
        ],
        compiler_params=pltpu.CompilerParams(
            dimension_semantics=("arbitrary",), vmem_limit_bytes=48 * 1024 * 1024
        ),
        cost_estimate=pl.CostEstimate(
            flops=flops, bytes_accessed=bytes_accessed, transcendentals=0
        ),
    )(tile_rows, tile_cols, live_count.reshape(1), tile_vals, row_blocks, col_blocks)


def exchange_pairs(size, step):
    return [(i, i ^ step) for i in range(size)]


def reversed_bits(value, bits):
    result = jnp.zeros_like(value)
    for k in range(bits):
        result = result | (((value >> k) & 1) << (bits - 1 - k))
    return result


def gather_blocks(local, axis):
    size = lax.axis_size(axis)
    held = local
    step = size // 2
    while step >= 1:
        held = jnp.concatenate([held, lax.ppermute(held, axis, exchange_pairs(size, step))], axis=0)
        step //= 2
    return held


def scatter_sum(totals, axis):
    size = lax.axis_size(axis)
    held = totals
    step = 1
    while step < size:
        half = held.shape[0] // 2
        sent = held[half:]
        if step == 1 and axis == "col":
            sent = sent.astype(jnp.bfloat16)
        held = held[:half] + lax.ppermute(sent, axis, exchange_pairs(size, step)).astype(held.dtype)
        step *= 2
    return held


def all_sum(value):
    for axis in ("row", "col"):
        size = lax.axis_size(axis)
        step = 1
        while step < size:
            value = value + lax.ppermute(value, axis, exchange_pairs(size, step))
            step *= 2
    return value


def held_position(index, axis, blocks_each):
    size = lax.axis_size(axis)
    bits = size.bit_length() - 1
    me = lax.axis_index(axis)
    owner = index // blocks_each
    return reversed_bits(me ^ owner, bits) * blocks_each + index % blocks_each


def to_blocks(vectors, tile):
    vec_width, local_nodes = vectors.shape
    return vectors.reshape(vec_width, local_nodes // tile, tile).transpose(1, 0, 2)


def from_blocks(blocks):
    count, vec_width, tile = blocks.shape
    return blocks.transpose(1, 0, 2).reshape(vec_width, count * tile)


def gathered(vectors, tile):
    local = to_blocks(vectors, tile)
    return gather_blocks(local, "col"), gather_blocks(local, "row")


def owned(row_totals, col_totals):
    return from_blocks(scatter_sum(row_totals, "col") + scatter_sum(col_totals, "row"))


def per_device(block_x, block_p, tile_rows, tile_cols, tile_count, tile_vals):
    highest = lax.Precision.HIGHEST
    width_k = block_x.shape[0]
    node_count = block_x.shape[1] * lax.axis_size("row") * lax.axis_size("col")
    blocks_each = block_x.shape[1] // tile_vals.shape[-1]
    slot_rows = held_position(tile_rows[0, 0], "col", blocks_each)
    slot_cols = held_position(tile_cols[0, 0], "row", blocks_each)
    live_count = tile_count[0, 0]
    slot_vals = tile_vals[0, 0]

    def product(left, right):
        return (
            jnp.dot(left, right.T, precision=highest, preferred_element_type=jnp.float32)
            / node_count
        )

    gram_x = all_sum(product(block_x, block_x))
    cholesky_factor = jnp.linalg.cholesky(gram_x)
    orthonormal = lax.linalg.triangular_solve(cholesky_factor, block_x, left_side=True, lower=True)
    tile = tile_vals.shape[-1]
    dir_rows, dir_cols = gathered(block_p.astype(jnp.bfloat16), tile)
    ortho_rows, ortho_cols = gathered(orthonormal.astype(jnp.bfloat16), tile)
    x_rows, x_cols, p_rows, p_cols = tile_products(
        jnp.concatenate([ortho_rows, dir_rows], axis=1),
        jnp.concatenate([ortho_cols, dir_cols], axis=1),
        slot_rows, slot_cols, live_count, slot_vals, (width_k, block_p.shape[0]),
    )
    image_x = owned(x_rows, x_cols)
    rayleigh = all_sum(product(orthonormal, image_x))
    residual = image_x - jnp.dot(
        rayleigh.T, orthonormal, precision=highest, preferred_element_type=jnp.float32
    )
    res_rows, res_cols = gathered(residual.astype(jnp.bfloat16), tile)
    image_p = owned(p_rows, p_cols)
    basis = jnp.concatenate([orthonormal, residual, block_p], axis=0)
    early = all_sum(
        jnp.concatenate(
            [product(basis, basis), product(basis, image_x), product(basis, image_p)], axis=1
        )
    )
    r_rows, r_cols = tile_products(
        res_rows, res_cols, slot_rows, slot_cols, live_count, slot_vals, (residual.shape[0],)
    )
    image_r = owned(r_rows, r_cols)
    late = all_sum(product(basis, image_r))
    span = basis.shape[0]
    gram_b = early[:, :span]
    gram_a = jnp.concatenate(
        [early[:, span:span + width_k], late, early[:, span + width_k:]], axis=1
    )
    return (residual, image_r, gram_a, gram_b)


def solution(mesh):
    in_specs = (
        P(None, ("row", "col")),
        P(None, ("row", "col")),
        P("row", "col", None),
        P("row", "col", None),
        P("row", "col"),
        P("row", "col", None, None, None),
    )
    out_specs = (P(None, ("row", "col")), P(None, ("row", "col")), P(), P())
    return jax.shard_map(
        per_device, mesh=mesh, in_specs=in_specs, out_specs=out_specs, check_vma=False
    )
```

```python
import functools

import jax
import jax.numpy as jnp
from jax import lax
from jax.experimental import pallas as pl
from jax.experimental.pallas import tpu as pltpu
from jax.sharding import PartitionSpec as P

GROUP = 64
UNROLL = 32


def tile_kernel(rows_ref, cols_ref, cnt_ref, vals_ref, rin_ref, cin_ref, *out_refs):
    g = pl.program_id(0)
    group = vals_ref.shape[0]
    row_outs = out_refs[0::2]
    col_outs = out_refs[1::2]
    edges = [0]
    for ref in row_outs:
        edges.append(edges[-1] + ref.shape[1])

    @pl.when(g == 0)
    def _():
        for ref in out_refs:
            ref[...] = jnp.zeros_like(ref)

    base = g * group
    live = cnt_ref[0]

    def tile_step(t):
        slot = base + t
        a = rows_ref[slot]
        b = cols_ref[slot]
        v = vals_ref[t]
        fwd = lax.dot_general(
            cin_ref[b], v, (((1,), (1,)), ((), ())), preferred_element_type=jnp.float32
        )
        bwd = jnp.dot(rin_ref[a], v, preferred_element_type=jnp.float32)
        for k in range(len(row_outs)):
            row_outs[k][a] += fwd[edges[k]:edges[k + 1]]
            col_outs[k][b] += bwd[edges[k]:edges[k + 1]]

    def full_body(t, carry):
        tile_step(t)
        return carry

    def part_body(t, carry):
        @pl.when(base + t < live)
        def _():
            tile_step(t)

        return carry

    @pl.when(base + group <= live)
    def _():
        lax.fori_loop(0, group, full_body, 0, unroll=UNROLL)

    @pl.when(jnp.logical_and(base < live, base + group > live))
    def _():
        lax.fori_loop(0, group, part_body, 0)


def tile_products(row_blocks, col_blocks, tile_rows, tile_cols, live_count, tile_vals, widths):
    n_rows, width, tile = row_blocks.shape
    n_cols = col_blocks.shape[0]
    slots = tile_vals.shape[0]
    group = GROUP if slots % GROUP == 0 else slots
    steps = slots // group

    def vals_map(g, rows, cols, cnt):
        last = jnp.maximum(cnt[0] - 1, 0) // group
        return (jnp.minimum(g, last), 0, 0)

    grid_spec = pltpu.PrefetchScalarGridSpec(
        num_scalar_prefetch=3,
        grid=(steps,),
        in_specs=[
            pl.BlockSpec((group, tile, tile), vals_map),
            pl.BlockSpec((n_rows, width, tile), lambda g, r, c, n: (0, 0, 0)),
            pl.BlockSpec((n_cols, width, tile), lambda g, r, c, n: (0, 0, 0)),
        ],
        out_specs=[
            pl.BlockSpec((n, w, tile), lambda g, r, c, k: (0, 0, 0))
            for w in widths
            for n in (n_rows, n_cols)
        ],
    )
    flops = 4 * slots * width * tile * tile
    bytes_accessed = (
        tile_vals.size * 2 + (row_blocks.size + col_blocks.size) * 2
        + (row_blocks.size + col_blocks.size) * 4
    )
    return pl.pallas_call(
        tile_kernel,
        grid_spec=grid_spec,
        out_shape=[
            jax.ShapeDtypeStruct((n, w, tile), jnp.float32) for w in widths for n in (n_rows, n_cols)
        ],
        compiler_params=pltpu.CompilerParams(
            dimension_semantics=("arbitrary",), vmem_limit_bytes=48 * 1024 * 1024
        ),
        cost_estimate=pl.CostEstimate(
            flops=flops, bytes_accessed=bytes_accessed, transcendentals=0
        ),
    )(tile_rows, tile_cols, live_count.reshape(1), tile_vals, row_blocks, col_blocks)


def exchange_pairs(size, step):
    return [(i, i ^ step) for i in range(size)]


def reversed_bits(value, bits):
    result = jnp.zeros_like(value)
    for k in range(bits):
        result = result | (((value >> k) & 1) << (bits - 1 - k))
    return result


def gather_blocks(local, axis):
    size = lax.axis_size(axis)
    held = local
    step = size // 2
    while step >= 1:
        held = jnp.concatenate([held, lax.ppermute(held, axis, exchange_pairs(size, step))], axis=0)
        step //= 2
    return held


def scatter_sum(totals, axis):
    size = lax.axis_size(axis)
    held = totals
    step = 1
    while step < size:
        half = held.shape[0] // 2
        sent = held[half:]
        if step == 1 and axis == "col":
            sent = sent.astype(jnp.bfloat16)
        held = held[:half] + lax.ppermute(sent, axis, exchange_pairs(size, step)).astype(held.dtype)
        step *= 2
    return held


def all_sum(value):
    for axis in ("row", "col"):
        size = lax.axis_size(axis)
        step = 1
        while step < size:
            value = value + lax.ppermute(value, axis, exchange_pairs(size, step))
            step *= 2
    return value


def all_sum_direct(value):
    for axis in ("row", "col"):
        size = lax.axis_size(axis)
        me = lax.axis_index(axis)
        got = [value] + [
            lax.ppermute(value, axis, exchange_pairs(size, step)) for step in range(1, size)
        ]
        ordered = jnp.take(jnp.stack(got), me ^ jnp.arange(size), axis=0)
        value = ordered[0]
        for k in range(1, size):
            value = value + ordered[k]
    return value


def held_position(index, axis, blocks_each):
    size = lax.axis_size(axis)
    bits = size.bit_length() - 1
    me = lax.axis_index(axis)
    owner = index // blocks_each
    return reversed_bits(me ^ owner, bits) * blocks_each + index % blocks_each


def to_blocks(vectors, tile):
    vec_width, local_nodes = vectors.shape
    return vectors.reshape(vec_width, local_nodes // tile, tile).transpose(1, 0, 2)


def from_blocks(blocks):
    count, vec_width, tile = blocks.shape
    return blocks.transpose(1, 0, 2).reshape(vec_width, count * tile)


def gathered(vectors, tile):
    local = to_blocks(vectors, tile)
    return gather_blocks(local, "col"), gather_blocks(local, "row")


def owned(row_totals, col_totals):
    return from_blocks(scatter_sum(row_totals, "col") + scatter_sum(col_totals, "row"))


def per_device(block_x, block_p, tile_rows, tile_cols, tile_count, tile_vals):
    highest = lax.Precision.HIGHEST
    width_k = block_x.shape[0]
    node_count = block_x.shape[1] * lax.axis_size("row") * lax.axis_size("col")
    blocks_each = block_x.shape[1] // tile_vals.shape[-1]
    slot_rows = held_position(tile_rows[0, 0], "col", blocks_each)
    slot_cols = held_position(tile_cols[0, 0], "row", blocks_each)
    live_count = tile_count[0, 0]
    slot_vals = tile_vals[0, 0]

    def product(left, right):
        return (
            jnp.dot(left, right.T, precision=highest, preferred_element_type=jnp.float32)
            / node_count
        )

    gram_x = all_sum_direct(product(block_x, block_x))
    cholesky_factor = jnp.linalg.cholesky(gram_x)
    orthonormal = lax.linalg.triangular_solve(cholesky_factor, block_x, left_side=True, lower=True)
    tile = tile_vals.shape[-1]
    dir_rows, dir_cols = gathered(block_p.astype(jnp.bfloat16), tile)
    ortho_rows, ortho_cols = gathered(orthonormal.astype(jnp.bfloat16), tile)
    x_rows, x_cols, p_rows, p_cols = tile_products(
        jnp.concatenate([ortho_rows, dir_rows], axis=1),
        jnp.concatenate([ortho_cols, dir_cols], axis=1),
        slot_rows, slot_cols, live_count, slot_vals, (width_k, block_p.shape[0]),
    )
    image_x = owned(x_rows, x_cols)
    rayleigh = all_sum_direct(product(orthonormal, image_x))
    residual = image_x - jnp.dot(
        rayleigh.T, orthonormal, precision=highest, preferred_element_type=jnp.float32
    )
    res_rows, res_cols = gathered(residual.astype(jnp.bfloat16), tile)
    image_p = owned(p_rows, p_cols)
    basis = jnp.concatenate([orthonormal, residual, block_p], axis=0)
    early = all_sum(
        jnp.concatenate(
            [product(basis, basis), product(basis, image_x), product(basis, image_p)], axis=1
        )
    )
    r_rows, r_cols = tile_products(
        res_rows, res_cols, slot_rows, slot_cols, live_count, slot_vals, (residual.shape[0],)
    )
    image_r = owned(r_rows, r_cols)
    late = all_sum_direct(product(basis, image_r))
    span = basis.shape[0]
    gram_b = early[:, :span]
    gram_a = jnp.concatenate(
        [early[:, span:span + width_k], late, early[:, span + width_k:]], axis=1
    )
    return (residual, image_r, gram_a, gram_b)


def solution(mesh):
    in_specs = (
        P(None, ("row", "col")),
        P(None, ("row", "col")),
        P("row", "col", None),
        P("row", "col", None),
        P("row", "col"),
        P("row", "col", None, None, None),
    )
    out_specs = (P(None, ("row", "col")), P(None, ("row", "col")), P(), P())
    return jax.shard_map(
        per_device, mesh=mesh, in_specs=in_specs, out_specs=out_specs, check_vma=False
    )
```

```python
import functools

import jax
import jax.numpy as jnp
from jax import lax
from jax.experimental import pallas as pl
from jax.experimental.pallas import tpu as pltpu
from jax.sharding import PartitionSpec as P

GROUP = 64
UNROLL = 64


def tile_kernel(rows_ref, cols_ref, cnt_ref, vals_ref, rin_ref, cin_ref, *out_refs):
    g = pl.program_id(0)
    group = vals_ref.shape[0]
    row_outs = out_refs[0::2]
    col_outs = out_refs[1::2]
    edges = [0]
    for ref in row_outs:
        edges.append(edges[-1] + ref.shape[1])

    @pl.when(g == 0)
    def _():
        for ref in out_refs:
            ref[...] = jnp.zeros_like(ref)

    base = g * group
    live = cnt_ref[0]

    def tile_step(t):
        slot = base + t
        a = rows_ref[slot]
        b = cols_ref[slot]
        v = vals_ref[t]
        fwd = lax.dot_general(
            cin_ref[b], v, (((1,), (1,)), ((), ())), preferred_element_type=jnp.float32
        )
        bwd = jnp.dot(rin_ref[a], v, preferred_element_type=jnp.float32)
        for k in range(len(row_outs)):
            row_outs[k][a] += fwd[edges[k]:edges[k + 1]]
            col_outs[k][b] += bwd[edges[k]:edges[k + 1]]

    def full_body(t, carry):
        tile_step(t)
        return carry

    def part_body(t, carry):
        @pl.when(base + t < live)
        def _():
            tile_step(t)

        return carry

    @pl.when(base + group <= live)
    def _():
        lax.fori_loop(0, group, full_body, 0, unroll=UNROLL)

    @pl.when(jnp.logical_and(base < live, base + group > live))
    def _():
        lax.fori_loop(0, group, part_body, 0)


def tile_products(row_blocks, col_blocks, tile_rows, tile_cols, live_count, tile_vals, widths):
    n_rows, width, tile = row_blocks.shape
    n_cols = col_blocks.shape[0]
    slots = tile_vals.shape[0]
    group = GROUP if slots % GROUP == 0 else slots
    steps = slots // group

    def vals_map(g, rows, cols, cnt):
        last = jnp.maximum(cnt[0] - 1, 0) // group
        return (jnp.minimum(g, last), 0, 0)

    grid_spec = pltpu.PrefetchScalarGridSpec(
        num_scalar_prefetch=3,
        grid=(steps,),
        in_specs=[
            pl.BlockSpec((group, tile, tile), vals_map),
            pl.BlockSpec((n_rows, width, tile), lambda g, r, c, n: (0, 0, 0)),
            pl.BlockSpec((n_cols, width, tile), lambda g, r, c, n: (0, 0, 0)),
        ],
        out_specs=[
            pl.BlockSpec((n, w, tile), lambda g, r, c, k: (0, 0, 0))
            for w in widths
            for n in (n_rows, n_cols)
        ],
    )
    flops = 4 * slots * width * tile * tile
    bytes_accessed = (
        tile_vals.size * 2 + (row_blocks.size + col_blocks.size) * 2
        + (row_blocks.size + col_blocks.size) * 4
    )
    return pl.pallas_call(
        tile_kernel,
        grid_spec=grid_spec,
        out_shape=[
            jax.ShapeDtypeStruct((n, w, tile), jnp.float32) for w in widths for n in (n_rows, n_cols)
        ],
        compiler_params=pltpu.CompilerParams(
            dimension_semantics=("arbitrary",), vmem_limit_bytes=48 * 1024 * 1024
        ),
        cost_estimate=pl.CostEstimate(
            flops=flops, bytes_accessed=bytes_accessed, transcendentals=0
        ),
    )(tile_rows, tile_cols, live_count.reshape(1), tile_vals, row_blocks, col_blocks)


def exchange_pairs(size, step):
    return [(i, i ^ step) for i in range(size)]


def reversed_bits(value, bits):
    result = jnp.zeros_like(value)
    for k in range(bits):
        result = result | (((value >> k) & 1) << (bits - 1 - k))
    return result


def gather_blocks(local, axis):
    size = lax.axis_size(axis)
    held = local
    step = size // 2
    while step >= 1:
        held = jnp.concatenate([held, lax.ppermute(held, axis, exchange_pairs(size, step))], axis=0)
        step //= 2
    return held


def scatter_sum(totals, axis):
    size = lax.axis_size(axis)
    held = totals
    step = 1
    while step < size:
        half = held.shape[0] // 2
        sent = held[half:]
        if step == 1 and axis == "col":
            sent = sent.astype(jnp.bfloat16)
        held = held[:half] + lax.ppermute(sent, axis, exchange_pairs(size, step)).astype(held.dtype)
        step *= 2
    return held


def all_sum(value):
    for axis in ("row", "col"):
        size = lax.axis_size(axis)
        step = 1
        while step < size:
            value = value + lax.ppermute(value, axis, exchange_pairs(size, step))
            step *= 2
    return value


def held_position(index, axis, blocks_each):
    size = lax.axis_size(axis)
    bits = size.bit_length() - 1
    me = lax.axis_index(axis)
    owner = index // blocks_each
    return reversed_bits(me ^ owner, bits) * blocks_each + index % blocks_each


def to_blocks(vectors, tile):
    vec_width, local_nodes = vectors.shape
    return vectors.reshape(vec_width, local_nodes // tile, tile).transpose(1, 0, 2)


def from_blocks(blocks):
    count, vec_width, tile = blocks.shape
    return blocks.transpose(1, 0, 2).reshape(vec_width, count * tile)


def gathered(vectors, tile):
    local = to_blocks(vectors, tile)
    return gather_blocks(local, "col"), gather_blocks(local, "row")


def owned(row_totals, col_totals):
    return from_blocks(scatter_sum(row_totals, "col") + scatter_sum(col_totals, "row"))


def per_device(block_x, block_p, tile_rows, tile_cols, tile_count, tile_vals):
    highest = lax.Precision.HIGHEST
    width_k = block_x.shape[0]
    node_count = block_x.shape[1] * lax.axis_size("row") * lax.axis_size("col")
    blocks_each = block_x.shape[1] // tile_vals.shape[-1]
    slot_rows = held_position(tile_rows[0, 0], "col", blocks_each)
    slot_cols = held_position(tile_cols[0, 0], "row", blocks_each)
    live_count = tile_count[0, 0]
    slot_vals = tile_vals[0, 0]

    def product(left, right):
        return (
            jnp.dot(left, right.T, precision=highest, preferred_element_type=jnp.float32)
            / node_count
        )

    gram_x = all_sum(product(block_x, block_x))
    cholesky_factor = jnp.linalg.cholesky(gram_x)
    orthonormal = lax.linalg.triangular_solve(cholesky_factor, block_x, left_side=True, lower=True)
    tile = tile_vals.shape[-1]
    dir_rows, dir_cols = gathered(block_p.astype(jnp.bfloat16), tile)
    p_rows, p_cols = tile_products(
        dir_rows, dir_cols, slot_rows, slot_cols, live_count, slot_vals, (block_p.shape[0],)
    )
    ortho_rows, ortho_cols = gathered(orthonormal.astype(jnp.bfloat16), tile)
    x_rows, x_cols = tile_products(
        ortho_rows, ortho_cols, slot_rows, slot_cols, live_count, slot_vals, (width_k,)
    )
    image_x = owned(x_rows, x_cols)
    rayleigh = all_sum(product(orthonormal, image_x))
    residual = image_x - jnp.dot(
        rayleigh.T, orthonormal, precision=highest, preferred_element_type=jnp.float32
    )
    res_rows, res_cols = gathered(residual.astype(jnp.bfloat16), tile)
    image_p = owned(p_rows, p_cols)
    basis = jnp.concatenate([orthonormal, residual, block_p], axis=0)
    early = all_sum(
        jnp.concatenate(
            [product(basis, basis), product(basis, image_x), product(basis, image_p)], axis=1
        )
    )
    r_rows, r_cols = tile_products(
        res_rows, res_cols, slot_rows, slot_cols, live_count, slot_vals, (residual.shape[0],)
    )
    image_r = owned(r_rows, r_cols)
    late = all_sum(product(basis, image_r))
    span = basis.shape[0]
    gram_b = early[:, :span]
    gram_a = jnp.concatenate(
        [early[:, span:span + width_k], late, early[:, span + width_k:]], axis=1
    )
    return (residual, image_r, gram_a, gram_b)


def solution(mesh):
    in_specs = (
        P(None, ("row", "col")),
        P(None, ("row", "col")),
        P("row", "col", None),
        P("row", "col", None),
        P("row", "col"),
        P("row", "col", None, None, None),
    )
    out_specs = (P(None, ("row", "col")), P(None, ("row", "col")), P(), P())
    return jax.shard_map(
        per_device, mesh=mesh, in_specs=in_specs, out_specs=out_specs, check_vma=False
    )
```

```python
import functools

import jax
import jax.numpy as jnp
from jax import lax
from jax.experimental import pallas as pl
from jax.experimental.pallas import tpu as pltpu
from jax.sharding import PartitionSpec as P

GROUP = 64
UNROLL = 64


def tile_kernel(rows_ref, cols_ref, cnt_ref, vals_ref, rin_ref, cin_ref, *out_refs):
    g = pl.program_id(0)
    group = vals_ref.shape[0]
    row_outs = out_refs[0::2]
    col_outs = out_refs[1::2]
    edges = [0]
    for ref in row_outs:
        edges.append(edges[-1] + ref.shape[1])

    @pl.when(g == 0)
    def _():
        for ref in out_refs:
            ref[...] = jnp.zeros_like(ref)

    base = g * group
    live = cnt_ref[0]

    def tile_step(t):
        slot = base + t
        a = rows_ref[slot]
        b = cols_ref[slot]
        v = vals_ref[t]
        fwd = lax.dot_general(
            cin_ref[b], v, (((1,), (1,)), ((), ())), preferred_element_type=jnp.float32
        )
        bwd = jnp.dot(rin_ref[a], v, preferred_element_type=jnp.float32)
        for k in range(len(row_outs)):
            row_outs[k][a] += fwd[edges[k]:edges[k + 1]]
            col_outs[k][b] += bwd[edges[k]:edges[k + 1]]

    def full_body(t, carry):
        tile_step(t)
        return carry

    def part_body(t, carry):
        @pl.when(base + t < live)
        def _():
            tile_step(t)

        return carry

    @pl.when(base + group <= live)
    def _():
        lax.fori_loop(0, group, full_body, 0, unroll=UNROLL)

    @pl.when(jnp.logical_and(base < live, base + group > live))
    def _():
        lax.fori_loop(0, group, part_body, 0)


def tile_products(row_blocks, col_blocks, tile_rows, tile_cols, live_count, tile_vals, widths):
    n_rows, width, tile = row_blocks.shape
    n_cols = col_blocks.shape[0]
    slots = tile_vals.shape[0]
    group = GROUP if slots % GROUP == 0 else slots
    steps = slots // group

    def vals_map(g, rows, cols, cnt):
        last = jnp.maximum(cnt[0] - 1, 0) // group
        return (jnp.minimum(g, last), 0, 0)

    grid_spec = pltpu.PrefetchScalarGridSpec(
        num_scalar_prefetch=3,
        grid=(steps,),
        in_specs=[
            pl.BlockSpec((group, tile, tile), vals_map),
            pl.BlockSpec((n_rows, width, tile), lambda g, r, c, n: (0, 0, 0)),
            pl.BlockSpec((n_cols, width, tile), lambda g, r, c, n: (0, 0, 0)),
        ],
        out_specs=[
            pl.BlockSpec((n, w, tile), lambda g, r, c, k: (0, 0, 0))
            for w in widths
            for n in (n_rows, n_cols)
        ],
    )
    flops = 4 * slots * width * tile * tile
    bytes_accessed = (
        tile_vals.size * 2 + (row_blocks.size + col_blocks.size) * 2
        + (row_blocks.size + col_blocks.size) * 4
    )
    return pl.pallas_call(
        tile_kernel,
        grid_spec=grid_spec,
        out_shape=[
            jax.ShapeDtypeStruct((n, w, tile), jnp.float32) for w in widths for n in (n_rows, n_cols)
        ],
        compiler_params=pltpu.CompilerParams(
            dimension_semantics=("arbitrary",), vmem_limit_bytes=48 * 1024 * 1024
        ),
        cost_estimate=pl.CostEstimate(
            flops=flops, bytes_accessed=bytes_accessed, transcendentals=0
        ),
    )(tile_rows, tile_cols, live_count.reshape(1), tile_vals, row_blocks, col_blocks)


def exchange_pairs(size, step):
    return [(i, i ^ step) for i in range(size)]


def reversed_bits(value, bits):
    result = jnp.zeros_like(value)
    for k in range(bits):
        result = result | (((value >> k) & 1) << (bits - 1 - k))
    return result


def gather_blocks(local, axis):
    size = lax.axis_size(axis)
    held = local
    step = size // 2
    while step >= 1:
        held = jnp.concatenate([held, lax.ppermute(held, axis, exchange_pairs(size, step))], axis=0)
        step //= 2
    return held


def scatter_sum(totals, axis):
    size = lax.axis_size(axis)
    held = totals
    step = 1
    while step < size:
        half = held.shape[0] // 2
        sent = held[half:]
        if step == 1 and axis == "col":
            sent = sent.astype(jnp.bfloat16)
        held = held[:half] + lax.ppermute(sent, axis, exchange_pairs(size, step)).astype(held.dtype)
        step *= 2
    return held


def all_sum(value):
    for axis in ("row", "col"):
        size = lax.axis_size(axis)
        step = 1
        while step < size:
            value = value + lax.ppermute(value, axis, exchange_pairs(size, step))
            step *= 2
    return value


def held_position(index, axis, blocks_each):
    size = lax.axis_size(axis)
    bits = size.bit_length() - 1
    me = lax.axis_index(axis)
    owner = index // blocks_each
    return reversed_bits(me ^ owner, bits) * blocks_each + index % blocks_each


def to_blocks(vectors, tile):
    vec_width, local_nodes = vectors.shape
    return vectors.reshape(vec_width, local_nodes // tile, tile).transpose(1, 0, 2)


def from_blocks(blocks):
    count, vec_width, tile = blocks.shape
    return blocks.transpose(1, 0, 2).reshape(vec_width, count * tile)


def gathered(vectors, tile):
    local = to_blocks(vectors, tile)
    return gather_blocks(local, "col"), gather_blocks(local, "row")


def owned(row_totals, col_totals):
    return from_blocks(scatter_sum(row_totals, "col") + scatter_sum(col_totals, "row"))


def per_device(block_x, block_p, tile_rows, tile_cols, tile_count, tile_vals):
    highest = lax.Precision.HIGHEST
    width_k = block_x.shape[0]
    node_count = block_x.shape[1] * lax.axis_size("row") * lax.axis_size("col")
    blocks_each = block_x.shape[1] // tile_vals.shape[-1]
    slot_rows = held_position(tile_rows[0, 0], "col", blocks_each)
    slot_cols = held_position(tile_cols[0, 0], "row", blocks_each)
    live_count = tile_count[0, 0]
    slot_vals = tile_vals[0, 0]

    def product(left, right):
        return (
            jnp.dot(left, right.T, precision=highest, preferred_element_type=jnp.float32)
            / node_count
        )

    gram_x = all_sum(product(block_x, block_x))
    cholesky_factor = jnp.linalg.cholesky(gram_x)
    orthonormal = lax.linalg.triangular_solve(cholesky_factor, block_x, left_side=True, lower=True)
    tile = tile_vals.shape[-1]
    dir_rows, dir_cols = gathered(block_p.astype(jnp.bfloat16), tile)
    ortho_rows, ortho_cols = gathered(orthonormal.astype(jnp.bfloat16), tile)
    x_rows, x_cols, p_rows, p_cols = tile_products(
        jnp.concatenate([ortho_rows, dir_rows], axis=1),
        jnp.concatenate([ortho_cols, dir_cols], axis=1),
        slot_rows, slot_cols, live_count, slot_vals, (width_k, block_p.shape[0]),
    )
    image_x = owned(x_rows, x_cols)
    rayleigh = all_sum(product(orthonormal, image_x))
    residual = image_x - jnp.dot(
        rayleigh.T, orthonormal, precision=highest, preferred_element_type=jnp.float32
    )
    res_rows, res_cols = gathered(residual.astype(jnp.bfloat16), tile)
    image_p = owned(p_rows, p_cols)
    basis = jnp.concatenate([orthonormal, residual, block_p], axis=0)
    early = all_sum(
        jnp.concatenate(
            [product(basis, basis), product(basis, image_x), product(basis, image_p)], axis=1
        )
    )
    r_rows, r_cols = tile_products(
        res_rows, res_cols, slot_rows, slot_cols, live_count, slot_vals, (residual.shape[0],)
    )
    image_r = owned(r_rows, r_cols)
    late = all_sum(product(basis, image_r))
    span = basis.shape[0]
    gram_b = early[:, :span]
    gram_a = jnp.concatenate(
        [early[:, span:span + width_k], late, early[:, span + width_k:]], axis=1
    )
    return (residual, image_r, gram_a, gram_b)


def solution(mesh):
    in_specs = (
        P(None, ("row", "col")),
        P(None, ("row", "col")),
        P("row", "col", None),
        P("row", "col", None),
        P("row", "col"),
        P("row", "col", None, None, None),
    )
    out_specs = (P(None, ("row", "col")), P(None, ("row", "col")), P(), P())
    return jax.shard_map(
        per_device, mesh=mesh, in_specs=in_specs, out_specs=out_specs, check_vma=False
    )
```
